512 devices in a mesh: seq: 64 (over z_lo, x, core), dp: 8 (over y, z_hi).
Axes of the slice: x: 4, y: 4, z: 16 (z_hi: 2, z_lo: 8; z = z_hi * 8 + z_lo), core: 2. Of those that a mesh axis runs over, the one named last changes fastest.
Arguments:
- queries: bfloat16 [65536, 2048], P(('dp', 'seq')), parts along dimension 0, may hold values from -20 to 20
- keys: bfloat16 [65536, 2048], P(('dp', 'seq')), parts along dimension 0, may hold values from -20 to 20
- values: bfloat16 [65536, 2048], P(('dp', 'seq')), parts along dimension 0, may hold values from -48 to 48
- cotangent: bfloat16 [65536, 2048], P(('dp', 'seq')), parts along dimension 0, may hold values from -24 to 24
- documents: int32 [65536], P(('dp', 'seq')), parts along dimension 0, may hold values from 0 to 7, never falling along the last dimension, each value on 1 to 6144 neighbouring positions
- global_offsets: int32 [1024], P(('dp', 'seq')), parts along dimension 0, may hold values from 0 to 127
Outputs:
- attended: bfloat16 [65536, 2048], P(('dp', 'seq')), parts along dimension 0
- query_grad: bfloat16 [65536, 2048], P(('dp', 'seq')), parts along dimension 0
- key_grad: bfloat16 [65536, 2048], P(('dp', 'seq')), parts along dimension 0
- value_grad: bfloat16 [65536, 2048], P(('dp', 'seq')), parts along dimension 0
The draws below stay inside these ranges and needn't reach their ends.
There are 8 independent parts, one for each index of `dp`. The reference program is written for one: setup_inputs(seed, part) draws one part's arguments, and reference() takes and returns one part's arrays. A program takes and returns all parts, laid end to end along the dimension named above; each array names one. Nothing has to cross between parts.
All inputs are finite; a program needn't handle non-finite values.
Results may differ from the reference program's by a relative error of at most 0.023.
Values may be sent and summed in bfloat16 or wider, within the bound.
No kernel may reach another device: no remote copies, remote signals or barrier semaphores. Data moves between devices by JAX's collectives and lax.ppermute only.
A program may use at most 64 MiB of HBM per device.

```python
import math
import jax
import jax.numpy as jnp
import numpy as np
from jax import lax

HEADS = 16
HD = 128
HH = 2048
TOK_DEV = 128
LEVELS = 2
GLOB_DEV = 2
DOCS = 8
SEQLEN = 8192
GLOBAL = 128
LONGEST = 6144
N_SEQ = 64


def draw_queries(key, part):
    drawn = jnp.clip(jax.random.normal(jax.random.fold_in(key, 1), (SEQLEN, HEADS * HD), jnp.float32), -5.0, 5.0)
    return drawn.astype(jnp.bfloat16)


def draw_keys(key, part):
    drawn = jnp.clip(jax.random.normal(jax.random.fold_in(key, 2), (SEQLEN, HEADS * HD), jnp.float32), -5.0, 5.0)
    return drawn.astype(jnp.bfloat16)


def place_ends(drawn, stream_key, low, high):
    extent = drawn.shape
    place = [jax.random.randint(jax.random.fold_in(stream_key, axis), (), 0, extent[axis]) for axis in range(len(extent))]
    drawn = drawn.at[tuple(place)].set(low)
    longest = extent.index(max(extent))
    place[longest] = (place[longest] + 1) % extent[longest]
    return drawn.at[tuple(place)].set(high)


def block_scale(key, dims, split, smallest, top_value):
    def one(dim, parts):
        draws = jax.random.uniform(jax.random.fold_in(jax.random.fold_in(key, 6), dim), (parts,), jnp.float32, smallest / len(split), top_value / len(split))
        return jnp.repeat(jnp.exp(draws), dims[dim] // parts).reshape((-1,) + (1,) * (len(dims) - dim - 1))

    loudness = one(*split[0])
    for cut in split[1:]:
        loudness = loudness * one(*cut)
    return loudness


def profile(amount, total, reach, skew):
    weights = [(1 << 20) // math.isqrt(rank ** skew) + 1 for rank in range(2, amount + 1)]
    surplus, given = total - reach - (amount - 1), [1] * (amount - 1)
    while surplus > 0:
        candidates = [i for i in range(amount - 1) if given[i] < reach]
        pool, budget = sum([weights[i] for i in candidates]), surplus
        for i in candidates:
            addition = min(reach - given[i], max(1, budget * weights[i] // pool), surplus)
            given[i] = given[i] + addition
            surplus = surplus - addition
    return np.array([reach] + given)


def ragged_sizes(key, amount, total, most, skew):
    if amount == 2:
        one = jax.random.randint(key, (), max(1, total - most), min(most, total - 1) + 1)
        return jnp.stack([one, total - one])
    tallies = jnp.asarray(profile(amount, total, most, skew), jnp.int32)
    pairs = (amount - 1) // 2
    donor, sink = tallies[1:1 + 2 * pairs:2], tallies[2:2 + 2 * pairs:2]
    room = jnp.minimum(donor - 1, most - sink)
    moved = jax.random.randint(jax.random.fold_in(key, 1), (pairs,), 0, 1 << 20) % (room + 1)
    tallies = tallies.at[1:1 + 2 * pairs:2].set(donor - moved).at[2:2 + 2 * pairs:2].set(sink + moved)
    return tallies[jax.random.permutation(jax.random.fold_in(key, 2), amount)]


def centred(stream_key, dims, scale, limit, shards=(), kind=jnp.bfloat16):
    entries = jax.random.normal(stream_key, dims, jnp.float32) * scale
    if len(shards) > 0:
        entries = block_scale(stream_key, dims, shards, -0.22, 0.18) * entries
    return jnp.clip(entries, min=-limit, max=limit).astype(kind)


def setup_inputs(seed: int = 0, part: int = 0) -> dict:
    key_list = jax.random.split(jax.random.key(seed), 7)
    part_splits = jax.random.split(jax.random.fold_in(key_list[6], part), 7)
    return {
        "queries": draw_queries(jax.random.fold_in(jax.random.fold_in(key_list[6], part), 71), part),
        "keys": draw_keys(jax.random.fold_in(jax.random.fold_in(key_list[6], part), 71), part),
        "values": centred(part_splits[2], (SEQLEN, HH), 8.0, 48.0, ((0, 64),)),
        "cotangent": centred(part_splits[3], (SEQLEN, HH), 4.0, 24.0, ((0, 64),)),
        "documents": jnp.searchsorted(jnp.cumsum(ragged_sizes(part_splits[4], DOCS, SEQLEN, LONGEST, 2)), jnp.arange(SEQLEN), side="right").astype(jnp.int32),
        "global_offsets": place_ends(jax.random.randint(part_splits[5], (GLOBAL,), 0, TOK_DEV), jax.random.fold_in(part_splits[5], 1), 0, TOK_DEV - 1).astype(jnp.int32),
    }


def rounded(source):
    return lax.optimization_barrier(source.astype(jnp.bfloat16)).astype(jnp.float32)


def reference(queries, keys, values, cotangent, documents, global_offsets):
    log_shards = N_SEQ.bit_length() - 1
    level_bits = [step * (log_shards - 2) // (LEVELS - 1) for step in range(LEVELS)]
    temper = HD ** -0.5
    blocks = jnp.arange(N_SEQ, dtype=jnp.int32)
    partners = [blocks] + [blocks ^ (1 << level_bit) for level_bit in level_bits]
    owners = jnp.arange(GLOBAL, dtype=jnp.int32) // GLOB_DEV
    global_rows = owners * TOK_DEV + global_offsets.astype(jnp.int32)
    distance = blocks[:, None] ^ owners[None, :]
    nearby = distance == 0
    for level_bit in level_bits:
        nearby = nearby | (distance == (1 << level_bit))
    far_mask = jnp.logical_not(nearby)
    doc_blocks = documents.reshape(N_SEQ, TOK_DEV)
    masks = [doc_blocks[:, :, None] == doc_blocks[partner][:, None, :] for partner in partners]

    def heads_first(array):
        return array.reshape(N_SEQ, TOK_DEV, HEADS, HD).transpose(2, 0, 1, 3)

    global_keys = keys[global_rows].reshape(GLOBAL, HEADS, HD).transpose(1, 0, 2)
    global_values = values[global_rows].reshape(GLOBAL, HEADS, HD).transpose(1, 0, 2)

    def one_head(inputs):
        query_rows, key_rows, value_rows, upstream, gkey, gvalue = [item.astype(jnp.float32) for item in inputs]
        scores = []
        for partner, mask in zip(partners, masks):
            raw = jnp.einsum('ntd,nud->ntu', query_rows, key_rows[partner]) * temper
            scores.append(jnp.where(mask, raw, -jnp.inf))
        global_scores = jnp.where(far_mask[:, None, :], jnp.einsum('ntd,gd->ntg', query_rows, gkey) * temper, -jnp.inf)
        highest = jnp.max(global_scores, axis=-1)
        for block_scores in scores:
            highest = jnp.maximum(highest, jnp.max(block_scores, axis=-1))
        exps = [jnp.exp(block_scores - highest[..., None]) for block_scores in scores]
        global_exp = jnp.exp(global_scores - highest[..., None])
        totals = jnp.sum(global_exp, axis=-1)
        for block_exp in exps:
            totals = totals + jnp.sum(block_exp, axis=-1)
        probs = [block_exp / totals[..., None] for block_exp in exps]
        global_prob = global_exp / totals[..., None]
        probs_b = [rounded(prob) for prob in probs]
        global_prob_b = rounded(global_prob)
        summed = jnp.einsum('ntg,gd->ntd', global_prob_b, gvalue)
        for partner, prob_b in zip(partners, probs_b):
            summed = summed + jnp.einsum('ntu,nud->ntd', prob_b, value_rows[partner])
        attended = summed.astype(jnp.bfloat16)
        delta = jnp.sum(upstream * attended.astype(jnp.float32), axis=-1)
        query_sum = jnp.zeros_like(query_rows)
        key_sum = jnp.zeros_like(query_rows)
        value_sum = jnp.zeros_like(query_rows)
        for group in range(LEVELS + 1):
            partner = partners[group]
            product = jnp.einsum('ntd,nud->ntu', upstream, value_rows[partner])
            slope = rounded(probs[group] * (product - delta[..., None]))
            query_sum = query_sum + jnp.einsum('ntu,nud->ntd', slope, key_rows[partner])
            key_part = temper * jnp.einsum('ntu,ntd->nud', slope, query_rows)
            value_part = jnp.einsum('ntu,ntd->nud', probs_b[group], upstream)
            if group == 0:
                key_sum = key_sum + key_part
                value_sum = value_sum + value_part
            else:
                key_sum = key_sum + rounded(key_part)[partner]
                value_sum = value_sum + rounded(value_part)[partner]
        global_product = jnp.einsum('ntd,gd->ntg', upstream, gvalue)
        global_slope = rounded(global_prob * (global_product - delta[..., None]))
        query_sum = query_sum + jnp.einsum('ntg,gd->ntd', global_slope, gkey)
        global_key_sum = temper * jnp.einsum('ntg,ntd->gd', global_slope, query_rows)
        global_value_sum = jnp.einsum('ntg,ntd->gd', global_prob_b, upstream)
        key_flat = key_sum.reshape(SEQLEN, HD).at[global_rows].add(global_key_sum)
        value_flat = value_sum.reshape(SEQLEN, HD).at[global_rows].add(global_value_sum)
        query_grad = (temper * query_sum).astype(jnp.bfloat16)
        return (attended.reshape(SEQLEN, HD), query_grad.reshape(SEQLEN, HD),
                key_flat.astype(jnp.bfloat16), value_flat.astype(jnp.bfloat16))

    results = lax.map(one_head, (heads_first(queries), heads_first(keys), heads_first(values),
                                 heads_first(cotangent), global_keys, global_values))

    def flatten(array):
        return array.transpose(1, 0, 2).reshape(SEQLEN, HEADS * HD)

    return (flatten(results[0]), flatten(results[1]), flatten(results[2]), flatten(results[3]))
```

```python
import jax
import jax.numpy as jnp
from jax import lax
from jax.sharding import PartitionSpec as P

HEADS = 16
LEVELS = 2


def from_partner(array, axis, stride):
    return lax.ppermute(array, axis, [(i, i ^ 1 << stride) for i in range(lax.axis_size(axis))])


def local(queries, keys, values, cotangent, documents, global_offsets):
    rows_here, columns = queries.shape
    head_size = columns // HEADS
    temper = head_size ** (-0.5)
    shards = lax.axis_size("seq")
    myself = lax.axis_index("seq")
    log_shards = shards.bit_length() - 1
    level_bits = [step * (log_shards - 2) // (LEVELS - 1) for step in range(LEVELS)]

    def split(array):
        return array.reshape(array.shape[0], HEADS, head_size)

    per_block = global_offsets.shape[0]
    picked = jnp.stack([keys[global_offsets], values[global_offsets]], 0)
    gather_bits = [5, 4, 2, 1, 3, 0] if log_shards == 6 else list(range(log_shards))[::-1]
    gathered = picked
    owner_bits = []
    for bit in gather_bits:
        came = from_partner(gathered, "seq", bit)
        upper = ((myself >> bit) & 1) == 1
        gathered = jnp.stack(
            [jnp.where(upper, came, gathered), jnp.where(upper, gathered, came)], 0
        )
        owner_bits.insert(0, bit)
    global_count = shards * per_block
    gathered = gathered.reshape((shards,) + picked.shape)
    global_keys = gathered[:, 0].reshape(global_count, columns)
    global_values = gathered[:, 1].reshape(global_count, columns)
    slot = jnp.arange(shards, dtype=jnp.int32)
    owners_perm = jnp.zeros_like(slot)
    for position, bit in enumerate(owner_bits):
        owners_perm = owners_perm | (((slot >> (log_shards - 1 - position)) & 1) << bit)
    owners = jnp.repeat(owners_perm, per_block)
    distance = owners ^ myself
    nearby = distance == 0
    for level_bit in level_bits:
        nearby = nearby | (distance == 1 << level_bit)
    query_heads = split(queries)
    dout_heads = split(cotangent)
    key_list = [keys]
    value_list = [values]
    mask_list = [documents[:, None] == documents[None, :]]
    for level_bit in level_bits:
        partner_keys, partner_values, partner_docs = from_partner(
            (keys, values, documents), "seq", level_bit
        )
        key_list.append(partner_keys)
        value_list.append(partner_values)
        mask_list.append(documents[:, None] == partner_docs[None, :])
    block_keys = jnp.concatenate(key_list, 0)
    block_values = jnp.concatenate(value_list, 0)
    block_mask = jnp.concatenate(mask_list, 1)
    raw = (
        jnp.einsum(
            "thd,uhd->htu", query_heads, split(block_keys), preferred_element_type=jnp.float32
        )
        * temper
    )
    block_scores = jnp.where(block_mask[None], raw, -jnp.inf)
    global_raw = (
        jnp.einsum(
            "thd,ghd->htg", query_heads, split(global_keys), preferred_element_type=jnp.float32
        )
        * temper
    )
    global_scores = jnp.where(jnp.logical_not(nearby)[None, None, :], global_raw, -jnp.inf)
    highest = jnp.maximum(jnp.max(global_scores, axis=-1), jnp.max(block_scores, axis=-1))
    block_exp = jnp.exp(block_scores - highest[..., None])
    global_exp = jnp.exp(global_scores - highest[..., None])
    totals = jnp.sum(global_exp, axis=-1) + jnp.sum(block_exp, axis=-1)
    probs = block_exp / totals[..., None]
    global_prob = global_exp / totals[..., None]
    probs_b = probs.astype(jnp.bfloat16)
    global_prob_b = global_prob.astype(jnp.bfloat16)
    summed = jnp.einsum(
        "htg,ghd->thd", global_prob_b, split(global_values), preferred_element_type=jnp.float32
    )
    summed = summed + jnp.einsum(
        "htu,uhd->thd", probs_b, split(block_values), preferred_element_type=jnp.float32
    )
    attended = summed.astype(jnp.bfloat16).reshape(rows_here, columns)
    delta = jnp.sum(dout_heads.astype(jnp.float32) * split(attended).astype(jnp.float32), axis=-1).T
    product = jnp.einsum(
        "thd,uhd->htu", dout_heads, split(block_values), preferred_element_type=jnp.float32
    )
    slope = (probs * (product - delta[:, :, None])).astype(jnp.bfloat16)
    query_term = jnp.einsum(
        "htu,uhd->thd", slope, split(block_keys), preferred_element_type=jnp.float32
    )
    key_term = temper * jnp.einsum(
        "htu,thd->uhd", slope, query_heads, preferred_element_type=jnp.float32
    )
    value_term = jnp.einsum("htu,thd->uhd", probs_b, dout_heads, preferred_element_type=jnp.float32)
    query_sum = query_term
    key_sum = key_term[:rows_here]
    value_sum = value_term[:rows_here]
    for level, level_bit in enumerate(level_bits):
        lower = (level + 1) * rows_here
        upper = (level + 2) * rows_here
        back_keys, back_values = from_partner(
            (
                key_term[lower:upper].reshape(rows_here, columns).astype(jnp.bfloat16),
                value_term[lower:upper].reshape(rows_here, columns).astype(jnp.bfloat16),
            ),
            "seq",
            level_bit,
        )
        key_sum = key_sum + split(back_keys).astype(jnp.float32)
        value_sum = value_sum + split(back_values).astype(jnp.float32)
    global_product = jnp.einsum(
        "thd,ghd->htg", dout_heads, split(global_values), preferred_element_type=jnp.float32
    )
    global_slope = (global_prob * (global_product - delta[:, :, None])).astype(jnp.bfloat16)
    query_sum = query_sum + jnp.einsum(
        "htg,ghd->thd", global_slope, split(global_keys), preferred_element_type=jnp.float32
    )
    key_part = temper * jnp.einsum(
        "htg,thd->ghd", global_slope, query_heads, preferred_element_type=jnp.float32
    )
    value_part = jnp.einsum(
        "htg,thd->ghd", global_prob_b, dout_heads, preferred_element_type=jnp.float32
    )
    owned = jnp.concatenate(
        [
            key_part.reshape(global_count, columns),
            value_part.reshape(global_count, columns),
        ],
        1,
    )
    for bit in owner_bits:
        owned = owned.reshape((2, -1) + owned.shape[1:])
        upper = ((myself >> bit) & 1) == 1
        keep = jnp.where(upper, owned[1], owned[0])
        send = jnp.where(upper, owned[0], owned[1])
        owned = keep + from_partner(send, "seq", bit)
    owned = owned.reshape(per_block, 2 * columns)
    placement = (jnp.arange(rows_here, dtype=jnp.int32)[:, None] == global_offsets[None, :]).astype(
        jnp.float32
    )
    spread_rows = jnp.dot(
        placement, owned, precision=lax.Precision.HIGHEST, preferred_element_type=jnp.float32
    )
    key_grad = (key_sum.reshape(rows_here, columns) + spread_rows[:, :columns]).astype(jnp.bfloat16)
    value_grad = (value_sum.reshape(rows_here, columns) + spread_rows[:, columns:]).astype(
        jnp.bfloat16
    )
    query_grad = (temper * query_sum).reshape(rows_here, columns).astype(jnp.bfloat16)
    return (attended, query_grad, key_grad, value_grad)


def solution(mesh):
    in_specs = (
        P(("dp", "seq"), None),
        P(("dp", "seq"), None),
        P(("dp", "seq"), None),
        P(("dp", "seq"), None),
        P(("dp", "seq")),
        P(("dp", "seq")),
    )
    out_specs = (
        P(("dp", "seq"), None),
        P(("dp", "seq"), None),
        P(("dp", "seq"), None),
        P(("dp", "seq"), None),
    )
    return jax.shard_map(local, mesh=mesh, in_specs=in_specs, out_specs=out_specs, check_vma=False)
```

```python
import jax
import jax.numpy as jnp
from jax import lax
from jax.sharding import PartitionSpec as P

HEADS = 16
LEVELS = 2


def from_partner(array, axis, stride):
    return lax.ppermute(array, axis, [(i, i ^ 1 << stride) for i in range(lax.axis_size(axis))])


def local(queries, keys, values, cotangent, documents, global_offsets):
    rows_here, columns = queries.shape
    head_size = columns // HEADS
    temper = head_size ** (-0.5)
    shards = lax.axis_size("seq")
    myself = lax.axis_index("seq")
    log_shards = shards.bit_length() - 1
    level_bits = [step * (log_shards - 2) // (LEVELS - 1) for step in range(LEVELS)]

    def split(array):
        return array.reshape(array.shape[0], HEADS, head_size)

    per_block = global_offsets.shape[0]
    picked = jnp.stack([keys[global_offsets], values[global_offsets]], 0)
    gather_bits = [5, 4, 2, 1, 3, 0] if log_shards == 6 else list(range(log_shards))[::-1]
    gathered = picked
    for bit in gather_bits:
        gathered = jnp.stack([gathered, from_partner(gathered, "seq", bit)], 0)
    owner_bits = gather_bits[::-1]
    global_count = shards * per_block
    gathered = gathered.reshape((shards,) + picked.shape)
    global_keys = gathered[:, 0].reshape(global_count, columns)
    global_values = gathered[:, 1].reshape(global_count, columns)
    slot = jnp.arange(shards, dtype=jnp.int32)
    distance = jnp.zeros_like(slot)
    for position, bit in enumerate(owner_bits):
        distance = distance | (((slot >> (log_shards - 1 - position)) & 1) << bit)
    distance = jnp.repeat(distance, per_block)
    nearby = distance == 0
    for level_bit in level_bits:
        nearby = nearby | (distance == 1 << level_bit)
    query_heads = split(queries)
    dout_heads = split(cotangent)
    key_list = [keys]
    value_list = [values]
    mask_list = [documents[:, None] == documents[None, :]]
    for level_bit in level_bits:
        partner_keys, partner_values, partner_docs = from_partner(
            (keys, values, documents), "seq", level_bit
        )
        key_list.append(partner_keys)
        value_list.append(partner_values)
        mask_list.append(documents[:, None] == partner_docs[None, :])
    block_keys = jnp.concatenate(key_list, 0)
    block_values = jnp.concatenate(value_list, 0)
    block_mask = jnp.concatenate(mask_list, 1)
    raw = (
        jnp.einsum(
            "thd,uhd->htu", query_heads, split(block_keys), preferred_element_type=jnp.float32
        )
        * temper
    )
    block_scores = jnp.where(block_mask[None], raw, -jnp.inf)
    global_raw = (
        jnp.einsum(
            "thd,ghd->htg", query_heads, split(global_keys), preferred_element_type=jnp.float32
        )
        * temper
    )
    global_scores = jnp.where(jnp.logical_not(nearby)[None, None, :], global_raw, -jnp.inf)
    highest = jnp.maximum(jnp.max(global_scores, axis=-1), jnp.max(block_scores, axis=-1))
    block_exp = jnp.exp(block_scores - highest[..., None])
    global_exp = jnp.exp(global_scores - highest[..., None])
    totals = jnp.sum(global_exp, axis=-1) + jnp.sum(block_exp, axis=-1)
    probs = block_exp / totals[..., None]
    global_prob = global_exp / totals[..., None]
    probs_b = probs.astype(jnp.bfloat16)
    global_prob_b = global_prob.astype(jnp.bfloat16)
    summed = jnp.einsum(
        "htg,ghd->thd", global_prob_b, split(global_values), preferred_element_type=jnp.float32
    )
    summed = summed + jnp.einsum(
        "htu,uhd->thd", probs_b, split(block_values), preferred_element_type=jnp.float32
    )
    attended = summed.astype(jnp.bfloat16).reshape(rows_here, columns)
    delta = jnp.sum(dout_heads.astype(jnp.float32) * split(attended).astype(jnp.float32), axis=-1).T
    product = jnp.einsum(
        "thd,uhd->htu", dout_heads, split(block_values), preferred_element_type=jnp.float32
    )
    slope = (probs * (product - delta[:, :, None])).astype(jnp.bfloat16)
    query_term = jnp.einsum(
        "htu,uhd->thd", slope, split(block_keys), preferred_element_type=jnp.float32
    )
    key_term = temper * jnp.einsum(
        "htu,thd->uhd", slope, query_heads, preferred_element_type=jnp.float32
    )
    value_term = jnp.einsum("htu,thd->uhd", probs_b, dout_heads, preferred_element_type=jnp.float32)
    query_sum = query_term
    key_sum = key_term[:rows_here]
    value_sum = value_term[:rows_here]
    for level, level_bit in enumerate(level_bits):
        lower = (level + 1) * rows_here
        upper = (level + 2) * rows_here
        back_keys, back_values = from_partner(
            (
                key_term[lower:upper].reshape(rows_here, columns).astype(jnp.bfloat16),
                value_term[lower:upper].reshape(rows_here, columns).astype(jnp.bfloat16),
            ),
            "seq",
            level_bit,
        )
        key_sum = key_sum + split(back_keys).astype(jnp.float32)
        value_sum = value_sum + split(back_values).astype(jnp.float32)
    global_product = jnp.einsum(
        "thd,ghd->htg", dout_heads, split(global_values), preferred_element_type=jnp.float32
    )
    global_slope = (global_prob * (global_product - delta[:, :, None])).astype(jnp.bfloat16)
    query_sum = query_sum + jnp.einsum(
        "htg,ghd->thd", global_slope, split(global_keys), preferred_element_type=jnp.float32
    )
    key_part = temper * jnp.einsum(
        "htg,thd->ghd", global_slope, query_heads, preferred_element_type=jnp.float32
    )
    value_part = jnp.einsum(
        "htg,thd->ghd", global_prob_b, dout_heads, preferred_element_type=jnp.float32
    )
    def scatter_rows(part):
        part = part.reshape(global_count, columns)
        for bit in owner_bits:
            half = part.shape[0] // 2
            part = part[:half] + from_partner(part[half:], "seq", bit)
        return part

    owned = jnp.concatenate([scatter_rows(key_part), scatter_rows(value_part)], 1)
    placement = (jnp.arange(rows_here, dtype=jnp.int32)[:, None] == global_offsets[None, :]).astype(
        jnp.float32
    )
    spread_rows = jnp.dot(
        placement, owned, precision=lax.Precision.HIGHEST, preferred_element_type=jnp.float32
    )
    key_grad = (key_sum.reshape(rows_here, columns) + spread_rows[:, :columns]).astype(jnp.bfloat16)
    value_grad = (value_sum.reshape(rows_here, columns) + spread_rows[:, columns:]).astype(
        jnp.bfloat16
    )
    query_grad = (temper * query_sum).reshape(rows_here, columns).astype(jnp.bfloat16)
    return (attended, query_grad, key_grad, value_grad)


def solution(mesh):
    in_specs = (
        P(("dp", "seq"), None),
        P(("dp", "seq"), None),
        P(("dp", "seq"), None),
        P(("dp", "seq"), None),
        P(("dp", "seq")),
        P(("dp", "seq")),
    )
    out_specs = (
        P(("dp", "seq"), None),
        P(("dp", "seq"), None),
        P(("dp", "seq"), None),
        P(("dp", "seq"), None),
    )
    return jax.shard_map(local, mesh=mesh, in_specs=in_specs, out_specs=out_specs, check_vma=False)
```

```python
import jax
import jax.numpy as jnp
from jax import lax
from jax.sharding import PartitionSpec as P

HEADS = 16
LEVELS = 2


def from_partner(array, axis, stride):
    return lax.ppermute(array, axis, [(i, i ^ 1 << stride) for i in range(lax.axis_size(axis))])


def body(queries, keys, values, cotangent, documents, global_offsets):
    rows_here, columns = queries.shape
    head_size = columns // HEADS
    temper = head_size ** (-0.5)
    shards = lax.axis_size("seq")
    log_shards = shards.bit_length() - 1
    level_bits = [step * (log_shards - 2) // (LEVELS - 1) for step in range(LEVELS)]

    def split(array):
        return array.reshape(array.shape[0], HEADS, head_size)

    per_block = global_offsets.shape[0]
    picked = jnp.stack([keys[global_offsets], values[global_offsets]], 0)
    gather_bits = list(range(log_shards))[::-1]
    z_steps = min(3, log_shards)
    doc_columns = 128
    packed = jnp.concatenate(
        [keys, values, jnp.broadcast_to(documents.astype(keys.dtype)[:, None], (rows_here, doc_columns))],
        1,
    )
    gathered = picked
    arrived = {}
    for step, bit in enumerate(gather_bits):
        gathered = jnp.stack([gathered, from_partner(gathered, "seq", bit)], 0)
        if step == z_steps - 1:
            gathered, held = lax.optimization_barrier((gathered, packed))
            for level_bit in level_bits:
                arrived[level_bit] = from_partner(held, "seq", level_bit)
    owner_bits = gather_bits[::-1]
    global_count = shards * per_block
    gathered = gathered.reshape((shards,) + picked.shape)
    global_keys = gathered[:, 0].reshape(global_count, columns)
    global_values = gathered[:, 1].reshape(global_count, columns)
    slot = jnp.arange(shards, dtype=jnp.int32)
    distance = jnp.zeros_like(slot)
    for position, bit in enumerate(owner_bits):
        distance = distance | (((slot >> (log_shards - 1 - position)) & 1) << bit)
    distance = jnp.repeat(distance, per_block)
    nearby = distance == 0
    for level_bit in level_bits:
        nearby = nearby | (distance == 1 << level_bit)
    query_heads = split(queries)
    dout_heads = split(cotangent)
    key_list = [keys]
    value_list = [values]
    mask_list = [documents[:, None] == documents[None, :]]
    for level_bit in level_bits:
        came = arrived[level_bit]
        partner_keys = came[:, :columns]
        partner_values = came[:, columns : 2 * columns]
        partner_docs = came[:, 2 * columns].astype(documents.dtype)
        key_list.append(partner_keys)
        value_list.append(partner_values)
        mask_list.append(documents[:, None] == partner_docs[None, :])
    block_keys = jnp.concatenate(key_list, 0)
    block_values = jnp.concatenate(value_list, 0)
    block_mask = jnp.concatenate(mask_list, 1)
    raw = (
        jnp.einsum(
            "thd,uhd->htu", query_heads, split(block_keys), preferred_element_type=jnp.float32
        )
        * temper
    )
    block_scores = jnp.where(block_mask[None], raw, -jnp.inf)
    global_raw = (
        jnp.einsum(
            "thd,ghd->htg", query_heads, split(global_keys), preferred_element_type=jnp.float32
        )
        * temper
    )
    global_scores = jnp.where(jnp.logical_not(nearby)[None, None, :], global_raw, -jnp.inf)
    highest = jnp.maximum(jnp.max(global_scores, axis=-1), jnp.max(block_scores, axis=-1))
    block_exp = jnp.exp(block_scores - highest[..., None])
    global_exp = jnp.exp(global_scores - highest[..., None])
    totals = jnp.sum(global_exp, axis=-1) + jnp.sum(block_exp, axis=-1)
    probs = block_exp / totals[..., None]
    global_prob = global_exp / totals[..., None]
    probs_b = probs.astype(jnp.bfloat16)
    global_prob_b = global_prob.astype(jnp.bfloat16)
    summed = jnp.einsum(
        "htg,ghd->thd", global_prob_b, split(global_values), preferred_element_type=jnp.float32
    )
    summed = summed + jnp.einsum(
        "htu,uhd->thd", probs_b, split(block_values), preferred_element_type=jnp.float32
    )
    attended = summed.astype(jnp.bfloat16).reshape(rows_here, columns)
    delta = jnp.sum(dout_heads.astype(jnp.float32) * split(attended).astype(jnp.float32), axis=-1).T
    product = jnp.einsum(
        "thd,uhd->htu", dout_heads, split(block_values), preferred_element_type=jnp.float32
    )
    slope = (probs * (product - delta[:, :, None])).astype(jnp.bfloat16)
    query_term = jnp.einsum(
        "htu,uhd->thd", slope, split(block_keys), preferred_element_type=jnp.float32
    )
    key_term = temper * jnp.einsum(
        "htu,thd->uhd", slope, query_heads, preferred_element_type=jnp.float32
    )
    value_term = jnp.einsum("htu,thd->uhd", probs_b, dout_heads, preferred_element_type=jnp.float32)
    query_sum = query_term
    key_sum = key_term[:rows_here]
    value_sum = value_term[:rows_here]
    for level, level_bit in enumerate(level_bits):
        lower = (level + 1) * rows_here
        upper = (level + 2) * rows_here
        back = from_partner(
            jnp.concatenate(
                [
                    key_term[lower:upper].reshape(rows_here, columns).astype(jnp.bfloat16),
                    value_term[lower:upper].reshape(rows_here, columns).astype(jnp.bfloat16),
                ],
                1,
            ),
            "seq",
            level_bit,
        )
        back_keys = back[:, :columns]
        back_values = back[:, columns:]
        key_sum = key_sum + split(back_keys).astype(jnp.float32)
        value_sum = value_sum + split(back_values).astype(jnp.float32)
    global_product = jnp.einsum(
        "thd,ghd->htg", dout_heads, split(global_values), preferred_element_type=jnp.float32
    )
    global_slope = (global_prob * (global_product - delta[:, :, None])).astype(jnp.bfloat16)
    query_sum = query_sum + jnp.einsum(
        "htg,ghd->thd", global_slope, split(global_keys), preferred_element_type=jnp.float32
    )
    key_part = temper * jnp.einsum(
        "htg,thd->ghd", global_slope, query_heads, preferred_element_type=jnp.float32
    )
    value_part = jnp.einsum(
        "htg,thd->ghd", global_prob_b, dout_heads, preferred_element_type=jnp.float32
    )
    owned = jnp.concatenate(
        [key_part.reshape(global_count, columns), value_part.reshape(global_count, columns)], 1
    )
    for bit in owner_bits:
        half = owned.shape[0] // 2
        owned = owned[:half] + from_partner(owned[half:], "seq", bit)
    placement = (jnp.arange(rows_here, dtype=jnp.int32)[:, None] == global_offsets[None, :]).astype(
        jnp.float32
    )
    spread_rows = jnp.dot(
        placement, owned, precision=lax.Precision.HIGHEST, preferred_element_type=jnp.float32
    )
    key_grad = (key_sum.reshape(rows_here, columns) + spread_rows[:, :columns]).astype(jnp.bfloat16)
    value_grad = (value_sum.reshape(rows_here, columns) + spread_rows[:, columns:]).astype(
        jnp.bfloat16
    )
    query_grad = (temper * query_sum).reshape(rows_here, columns).astype(jnp.bfloat16)
    return (attended, query_grad, key_grad, value_grad)


def solution(mesh):
    in_specs = (
        P(("dp", "seq"), None),
        P(("dp", "seq"), None),
        P(("dp", "seq"), None),
        P(("dp", "seq"), None),
        P(("dp", "seq")),
        P(("dp", "seq")),
    )
    out_specs = (
        P(("dp", "seq"), None),
        P(("dp", "seq"), None),
        P(("dp", "seq"), None),
        P(("dp", "seq"), None),
    )
    return jax.shard_map(body, mesh=mesh, in_specs=in_specs, out_specs=out_specs, check_vma=False)
```

```python
import jax
import jax.numpy as jnp
from jax import lax
from jax.sharding import PartitionSpec as P

HEADS = 16
LEVELS = 2


def from_partner(array, axis, stride):
    return lax.ppermute(array, axis, [(i, i ^ 1 << stride) for i in range(lax.axis_size(axis))])


def body(queries, keys, values, cotangent, documents, global_offsets):
    rows_here, columns = queries.shape
    head_size = columns // HEADS
    temper = head_size ** (-0.5)
    shards = lax.axis_size("seq")
    log_shards = shards.bit_length() - 1
    level_bits = [step * (log_shards - 2) // (LEVELS - 1) for step in range(LEVELS)]

    def split(array):
        return array.reshape(array.shape[0], HEADS, head_size)

    per_block = global_offsets.shape[0]
    picked = jnp.stack([keys[global_offsets], values[global_offsets]], 0)
    gather_bits = list(range(log_shards))[::-1]
    z_steps = min(3, log_shards)
    doc_columns = 128
    packed = jnp.concatenate(
        [keys, values, jnp.broadcast_to(documents.astype(keys.dtype)[:, None], (rows_here, doc_columns))],
        1,
    )
    gathered = picked
    arrived = {}
    for step, bit in enumerate(gather_bits):
        gathered = jnp.stack([gathered, from_partner(gathered, "seq", bit)], 0)
        if step == z_steps - 1:
            gathered, held = lax.optimization_barrier((gathered, packed))
            for level_bit in level_bits:
                arrived[level_bit] = from_partner(held, "seq", level_bit)
    owner_bits = gather_bits[::-1]
    global_count = shards * per_block
    gathered = gathered.reshape((shards,) + picked.shape)
    global_keys = gathered[:, 0].reshape(global_count, columns)
    global_values = gathered[:, 1].reshape(global_count, columns)
    slot = jnp.arange(shards, dtype=jnp.int32)
    distance = jnp.zeros_like(slot)
    for position, bit in enumerate(owner_bits):
        distance = distance | (((slot >> (log_shards - 1 - position)) & 1) << bit)
    distance = jnp.repeat(distance, per_block)
    nearby = distance == 0
    for level_bit in level_bits:
        nearby = nearby | (distance == 1 << level_bit)
    query_heads = split(queries)
    dout_heads = split(cotangent)
    key_list = [keys]
    value_list = [values]
    mask_list = [documents[:, None] == documents[None, :]]
    for level_bit in level_bits:
        came = arrived[level_bit]
        partner_keys = came[:, :columns]
        partner_values = came[:, columns : 2 * columns]
        partner_docs = came[:, 2 * columns].astype(documents.dtype)
        key_list.append(partner_keys)
        value_list.append(partner_values)
        mask_list.append(documents[:, None] == partner_docs[None, :])
    block_keys = jnp.concatenate(key_list, 0)
    block_values = jnp.concatenate(value_list, 0)
    block_mask = jnp.concatenate(mask_list, 1)
    raw = (
        jnp.einsum(
            "thd,uhd->htu", query_heads, split(block_keys), preferred_element_type=jnp.float32
        )
        * temper
    )
    block_scores = jnp.where(block_mask[None], raw, -jnp.inf)
    global_raw = (
        jnp.einsum(
            "thd,ghd->htg", query_heads, split(global_keys), preferred_element_type=jnp.float32
        )
        * temper
    )
    global_scores = jnp.where(jnp.logical_not(nearby)[None, None, :], global_raw, -jnp.inf)
    highest = jnp.maximum(jnp.max(global_scores, axis=-1), jnp.max(block_scores, axis=-1))
    block_exp = jnp.exp(block_scores - highest[..., None])
    global_exp = jnp.exp(global_scores - highest[..., None])
    totals = jnp.sum(global_exp, axis=-1) + jnp.sum(block_exp, axis=-1)
    probs = block_exp / totals[..., None]
    global_prob = global_exp / totals[..., None]
    probs_b = probs.astype(jnp.bfloat16)
    global_prob_b = global_prob.astype(jnp.bfloat16)
    summed = jnp.einsum(
        "htg,ghd->thd", global_prob_b, split(global_values), preferred_element_type=jnp.float32
    )
    summed = summed + jnp.einsum(
        "htu,uhd->thd", probs_b, split(block_values), preferred_element_type=jnp.float32
    )
    attended = summed.astype(jnp.bfloat16).reshape(rows_here, columns)
    delta = jnp.sum(dout_heads.astype(jnp.float32) * split(attended).astype(jnp.float32), axis=-1).T
    product = jnp.einsum(
        "thd,uhd->htu", dout_heads, split(block_values), preferred_element_type=jnp.float32
    )
    slope = (probs * (product - delta[:, :, None])).astype(jnp.bfloat16)
    query_term = jnp.einsum(
        "htu,uhd->thd", slope, split(block_keys), preferred_element_type=jnp.float32
    )
    key_term = temper * jnp.einsum(
        "htu,thd->uhd", slope, query_heads, preferred_element_type=jnp.float32
    )
    value_term = jnp.einsum("htu,thd->uhd", probs_b, dout_heads, preferred_element_type=jnp.float32)
    query_sum = query_term
    key_sum = key_term[:rows_here]
    value_sum = value_term[:rows_here]
    for level, level_bit in enumerate(level_bits):
        lower = (level + 1) * rows_here
        upper = (level + 2) * rows_here
        key_back = key_term[lower:upper].reshape(rows_here, columns).astype(jnp.bfloat16)
        value_back = value_term[lower:upper].reshape(rows_here, columns).astype(jnp.bfloat16)
        if level_bit == 0:
            back = from_partner(jnp.concatenate([key_back, value_back], 1), "seq", level_bit)
            back_keys = back[:, :columns]
            back_values = back[:, columns:]
        else:
            back_values = from_partner(value_back, "seq", level_bit)
            back_keys = from_partner(key_back, "seq", level_bit)
        key_sum = key_sum + split(back_keys).astype(jnp.float32)
        value_sum = value_sum + split(back_values).astype(jnp.float32)
    global_product = jnp.einsum(
        "thd,ghd->htg", dout_heads, split(global_values), preferred_element_type=jnp.float32
    )
    global_slope = (global_prob * (global_product - delta[:, :, None])).astype(jnp.bfloat16)
    query_sum = query_sum + jnp.einsum(
        "htg,ghd->thd", global_slope, split(global_keys), preferred_element_type=jnp.float32
    )
    key_part = temper * jnp.einsum(
        "htg,thd->ghd", global_slope, query_heads, preferred_element_type=jnp.float32
    )
    value_part = jnp.einsum(
        "htg,thd->ghd", global_prob_b, dout_heads, preferred_element_type=jnp.float32
    )
    owned = jnp.concatenate(
        [key_part.reshape(global_count, columns), value_part.reshape(global_count, columns)], 1
    )
    for bit in owner_bits:
        half = owned.shape[0] // 2
        owned = owned[:half] + from_partner(owned[half:], "seq", bit)
    placement = (jnp.arange(rows_here, dtype=jnp.int32)[:, None] == global_offsets[None, :]).astype(
        jnp.float32
    )
    spread_rows = jnp.dot(
        placement, owned, precision=lax.Precision.HIGHEST, preferred_element_type=jnp.float32
    )
    key_grad = (key_sum.reshape(rows_here, columns) + spread_rows[:, :columns]).astype(jnp.bfloat16)
    value_grad = (value_sum.reshape(rows_here, columns) + spread_rows[:, columns:]).astype(
        jnp.bfloat16
    )
    query_grad = (temper * query_sum).reshape(rows_here, columns).astype(jnp.bfloat16)
    return (attended, query_grad, key_grad, value_grad)


def solution(mesh):
    in_specs = (
        P(("dp", "seq"), None),
        P(("dp", "seq"), None),
        P(("dp", "seq"), None),
        P(("dp", "seq"), None),
        P(("dp", "seq")),
        P(("dp", "seq")),
    )
    out_specs = (
        P(("dp", "seq"), None),
        P(("dp", "seq"), None),
        P(("dp", "seq"), None),
        P(("dp", "seq"), None),
    )
    return jax.shard_map(body, mesh=mesh, in_specs=in_specs, out_specs=out_specs, check_vma=False)
```

```python
import jax
import jax.numpy as jnp
from jax import lax
from jax.sharding import PartitionSpec as P

HEADS = 16
LEVELS = 2


def from_partner(array, axis, stride):
    return lax.ppermute(array, axis, [(i, i ^ 1 << stride) for i in range(lax.axis_size(axis))])


def body(queries, keys, values, cotangent, documents, global_offsets):
    rows_here, columns = queries.shape
    head_size = columns // HEADS
    temper = head_size ** (-0.5)
    shards = lax.axis_size("seq")
    log_shards = shards.bit_length() - 1
    level_bits = [step * (log_shards - 2) // (LEVELS - 1) for step in range(LEVELS)]

    def split(array):
        return array.reshape(array.shape[0], HEADS, head_size)

    per_block = global_offsets.shape[0]
    picked = jnp.stack([keys[global_offsets], values[global_offsets]], 0)
    gather_bits = list(range(log_shards))[::-1]
    z_steps = min(3, log_shards)
    doc_columns = 128
    packed = jnp.concatenate(
        [keys, values, jnp.broadcast_to(documents.astype(keys.dtype)[:, None], (rows_here, doc_columns))],
        1,
    )
    gathered = picked
    arrived = {}
    for step, bit in enumerate(gather_bits):
        gathered = jnp.stack([gathered, from_partner(gathered, "seq", bit)], 0)
        if step == z_steps - 1:
            gathered, held = lax.optimization_barrier((gathered, packed))
            for level_bit in level_bits:
                if level_bit == 0:
                    came = from_partner(held, "seq", level_bit)
                    arrived[level_bit] = (
                        came[:, :columns],
                        came[:, columns : 2 * columns],
                        came[:, 2 * columns],
                    )
                    continue
                first = from_partner(
                    jnp.concatenate([held[:, :columns], held[:, 2 * columns :]], 1),
                    "seq",
                    level_bit,
                )
                second = from_partner(held[:, columns : 2 * columns], "seq", level_bit)
                arrived[level_bit] = (first[:, :columns], second, first[:, columns])
    owner_bits = gather_bits[::-1]
    global_count = shards * per_block
    gathered = gathered.reshape((shards,) + picked.shape)
    global_keys = gathered[:, 0].reshape(global_count, columns)
    global_values = gathered[:, 1].reshape(global_count, columns)
    slot = jnp.arange(shards, dtype=jnp.int32)
    distance = jnp.zeros_like(slot)
    for position, bit in enumerate(owner_bits):
        distance = distance | (((slot >> (log_shards - 1 - position)) & 1) << bit)
    distance = jnp.repeat(distance, per_block)
    nearby = distance == 0
    for level_bit in level_bits:
        nearby = nearby | (distance == 1 << level_bit)
    query_heads = split(queries)
    dout_heads = split(cotangent)
    key_list = [keys]
    value_list = [values]
    mask_list = [documents[:, None] == documents[None, :]]
    for level_bit in level_bits:
        partner_keys, partner_values, partner_docs = arrived[level_bit]
        partner_docs = partner_docs.astype(documents.dtype)
        key_list.append(partner_keys)
        value_list.append(partner_values)
        mask_list.append(documents[:, None] == partner_docs[None, :])
    block_keys = jnp.concatenate(key_list, 0)
    block_values = jnp.concatenate(value_list, 0)
    block_mask = jnp.concatenate(mask_list, 1)
    raw = (
        jnp.einsum(
            "thd,uhd->htu", query_heads, split(block_keys), preferred_element_type=jnp.float32
        )
        * temper
    )
    block_scores = jnp.where(block_mask[None], raw, -jnp.inf)
    global_raw = (
        jnp.einsum(
            "thd,ghd->htg", query_heads, split(global_keys), preferred_element_type=jnp.float32
        )
        * temper
    )
    global_scores = jnp.where(jnp.logical_not(nearby)[None, None, :], global_raw, -jnp.inf)
    highest = jnp.maximum(jnp.max(global_scores, axis=-1), jnp.max(block_scores, axis=-1))
    block_exp = jnp.exp(block_scores - highest[..., None])
    global_exp = jnp.exp(global_scores - highest[..., None])
    totals = jnp.sum(global_exp, axis=-1) + jnp.sum(block_exp, axis=-1)
    probs = block_exp / totals[..., None]
    global_prob = global_exp / totals[..., None]
    probs_b = probs.astype(jnp.bfloat16)
    global_prob_b = global_prob.astype(jnp.bfloat16)
    summed = jnp.einsum(
        "htg,ghd->thd", global_prob_b, split(global_values), preferred_element_type=jnp.float32
    )
    summed = summed + jnp.einsum(
        "htu,uhd->thd", probs_b, split(block_values), preferred_element_type=jnp.float32
    )
    attended = summed.astype(jnp.bfloat16).reshape(rows_here, columns)
    delta = jnp.sum(dout_heads.astype(jnp.float32) * split(attended).astype(jnp.float32), axis=-1).T
    product = jnp.einsum(
        "thd,uhd->htu", dout_heads, split(block_values), preferred_element_type=jnp.float32
    )
    slope = (probs * (product - delta[:, :, None])).astype(jnp.bfloat16)
    query_term = jnp.einsum(
        "htu,uhd->thd", slope, split(block_keys), preferred_element_type=jnp.float32
    )
    key_term = temper * jnp.einsum(
        "htu,thd->uhd", slope, query_heads, preferred_element_type=jnp.float32
    )
    value_term = jnp.einsum("htu,thd->uhd", probs_b, dout_heads, preferred_element_type=jnp.float32)
    query_sum = query_term
    key_sum = key_term[:rows_here]
    value_sum = value_term[:rows_here]
    for level, level_bit in enumerate(level_bits):
        lower = (level + 1) * rows_here
        upper = (level + 2) * rows_here
        key_back = key_term[lower:upper].reshape(rows_here, columns).astype(jnp.bfloat16)
        value_back = value_term[lower:upper].reshape(rows_here, columns).astype(jnp.bfloat16)
        if level_bit == 0:
            back = from_partner(jnp.concatenate([key_back, value_back], 1), "seq", level_bit)
            back_keys = back[:, :columns]
            back_values = back[:, columns:]
        else:
            back_values = from_partner(value_back, "seq", level_bit)
            back_keys = from_partner(key_back, "seq", level_bit)
        key_sum = key_sum + split(back_keys).astype(jnp.float32)
        value_sum = value_sum + split(back_values).astype(jnp.float32)
    global_product = jnp.einsum(
        "thd,ghd->htg", dout_heads, split(global_values), preferred_element_type=jnp.float32
    )
    global_slope = (global_prob * (global_product - delta[:, :, None])).astype(jnp.bfloat16)
    query_sum = query_sum + jnp.einsum(
        "htg,ghd->thd", global_slope, split(global_keys), preferred_element_type=jnp.float32
    )
    key_part = temper * jnp.einsum(
        "htg,thd->ghd", global_slope, query_heads, preferred_element_type=jnp.float32
    )
    value_part = jnp.einsum(
        "htg,thd->ghd", global_prob_b, dout_heads, preferred_element_type=jnp.float32
    )
    owned = jnp.concatenate(
        [key_part.reshape(global_count, columns), value_part.reshape(global_count, columns)], 1
    )
    for bit in owner_bits:
        half = owned.shape[0] // 2
        sent = owned[half:].astype(jnp.bfloat16)
        owned = owned[:half] + from_partner(sent, "seq", bit).astype(jnp.float32)
    placement = (jnp.arange(rows_here, dtype=jnp.int32)[:, None] == global_offsets[None, :]).astype(
        jnp.float32
    )
    spread_rows = jnp.dot(
        placement, owned, precision=lax.Precision.HIGHEST, preferred_element_type=jnp.float32
    )
    key_grad = (key_sum.reshape(rows_here, columns) + spread_rows[:, :columns]).astype(jnp.bfloat16)
    value_grad = (value_sum.reshape(rows_here, columns) + spread_rows[:, columns:]).astype(
        jnp.bfloat16
    )
    query_grad = (temper * query_sum).reshape(rows_here, columns).astype(jnp.bfloat16)
    return (attended, query_grad, key_grad, value_grad)


def solution(mesh):
    in_specs = (
        P(("dp", "seq"), None),
        P(("dp", "seq"), None),
        P(("dp", "seq"), None),
        P(("dp", "seq"), None),
        P(("dp", "seq")),
        P(("dp", "seq")),
    )
    out_specs = (
        P(("dp", "seq"), None),
        P(("dp", "seq"), None),
        P(("dp", "seq"), None),
        P(("dp", "seq"), None),
    )
    return jax.shard_map(body, mesh=mesh, in_specs=in_specs, out_specs=out_specs, check_vma=False)
```

```python
import jax
import jax.numpy as jnp
from jax import lax
from jax.sharding import PartitionSpec as P

HEADS = 16
LEVELS = 2


def from_partner(array, axis, stride):
    return lax.ppermute(array, axis, [(i, i ^ 1 << stride) for i in range(lax.axis_size(axis))])


def body(queries, keys, values, cotangent, documents, global_offsets):
    rows_here, columns = queries.shape
    head_size = columns // HEADS
    temper = head_size ** (-0.5)
    shards = lax.axis_size("seq")
    log_shards = shards.bit_length() - 1
    level_bits = [step * (log_shards - 2) // (LEVELS - 1) for step in range(LEVELS)]

    def split(array):
        return array.reshape(array.shape[0], HEADS, head_size)

    per_block = global_offsets.shape[0]
    picked = jnp.stack([keys[global_offsets], values[global_offsets]], 0)
    gather_bits = list(range(log_shards))[::-1]
    z_steps = min(3, log_shards)
    doc_columns = 128
    packed = jnp.concatenate(
        [keys, values, jnp.broadcast_to(documents.astype(keys.dtype)[:, None], (rows_here, doc_columns))],
        1,
    )
    gathered = picked
    arrived = {}
    for step, bit in enumerate(gather_bits):
        gathered = jnp.stack([gathered, from_partner(gathered, "seq", bit)], 0)
        if step == z_steps - 1:
            gathered, held = lax.optimization_barrier((gathered, packed))
            for level_bit in level_bits:
                arrived[level_bit] = from_partner(held, "seq", level_bit)
    owner_bits = gather_bits[::-1]
    global_count = shards * per_block
    gathered = gathered.reshape((shards,) + picked.shape)
    global_keys = gathered[:, 0].reshape(global_count, columns)
    global_values = gathered[:, 1].reshape(global_count, columns)
    slot = jnp.arange(shards, dtype=jnp.int32)
    distance = jnp.zeros_like(slot)
    for position, bit in enumerate(owner_bits):
        distance = distance | (((slot >> (log_shards - 1 - position)) & 1) << bit)
    distance = jnp.repeat(distance, per_block)
    nearby = distance == 0
    for level_bit in level_bits:
        nearby = nearby | (distance == 1 << level_bit)
    query_heads = split(queries)
    dout_heads = split(cotangent)
    key_list = [keys]
    value_list = [values]
    mask_list = [documents[:, None] == documents[None, :]]
    for level_bit in level_bits:
        came = arrived[level_bit]
        partner_keys = came[:, :columns]
        partner_values = came[:, columns : 2 * columns]
        partner_docs = came[:, 2 * columns].astype(documents.dtype)
        key_list.append(partner_keys)
        value_list.append(partner_values)
        mask_list.append(documents[:, None] == partner_docs[None, :])
    block_keys = jnp.concatenate(key_list, 0)
    block_values = jnp.concatenate(value_list, 0)
    block_mask = jnp.concatenate(mask_list, 1)
    raws = [
        jnp.einsum("thd,uhd->htu", query_heads, split(group), preferred_element_type=jnp.float32)
        for group in key_list
    ]
    products = [
        jnp.einsum("thd,uhd->htu", dout_heads, split(group), preferred_element_type=jnp.float32)
        for group in value_list
    ]
    early = [0] + [level + 1 for level, level_bit in enumerate(level_bits) if level_bit == 0]
    held = lax.optimization_barrier(([raws[i] for i in early], [products[i] for i in early]))
    for position, i in enumerate(early):
        raws[i] = held[0][position]
        products[i] = held[1][position]
    raw = jnp.concatenate(raws, 2) * temper
    block_scores = jnp.where(block_mask[None], raw, -jnp.inf)
    global_raw = (
        jnp.einsum(
            "thd,ghd->htg", query_heads, split(global_keys), preferred_element_type=jnp.float32
        )
        * temper
    )
    global_scores = jnp.where(jnp.logical_not(nearby)[None, None, :], global_raw, -jnp.inf)
    highest = jnp.maximum(jnp.max(global_scores, axis=-1), jnp.max(block_scores, axis=-1))
    block_exp = jnp.exp(block_scores - highest[..., None])
    global_exp = jnp.exp(global_scores - highest[..., None])
    totals = jnp.sum(global_exp, axis=-1) + jnp.sum(block_exp, axis=-1)
    probs = block_exp / totals[..., None]
    global_prob = global_exp / totals[..., None]
    probs_b = probs.astype(jnp.bfloat16)
    global_prob_b = global_prob.astype(jnp.bfloat16)
    summed = jnp.einsum(
        "htg,ghd->thd", global_prob_b, split(global_values), preferred_element_type=jnp.float32
    )
    summed = summed + jnp.einsum(
        "htu,uhd->thd", probs_b, split(block_values), preferred_element_type=jnp.float32
    )
    attended = summed.astype(jnp.bfloat16).reshape(rows_here, columns)
    delta = jnp.sum(dout_heads.astype(jnp.float32) * split(attended).astype(jnp.float32), axis=-1).T
    product = jnp.concatenate(products, 2)
    slope = (probs * (product - delta[:, :, None])).astype(jnp.bfloat16)
    query_term = jnp.einsum(
        "htu,uhd->thd", slope, split(block_keys), preferred_element_type=jnp.float32
    )
    key_term = temper * jnp.einsum(
        "htu,thd->uhd", slope, query_heads, preferred_element_type=jnp.float32
    )
    value_term = jnp.einsum("htu,thd->uhd", probs_b, dout_heads, preferred_element_type=jnp.float32)
    query_sum = query_term
    key_sum = key_term[:rows_here]
    value_sum = value_term[:rows_here]
    for level, level_bit in enumerate(level_bits):
        lower = (level + 1) * rows_here
        upper = (level + 2) * rows_here
        key_back = key_term[lower:upper].reshape(rows_here, columns).astype(jnp.bfloat16)
        value_back = value_term[lower:upper].reshape(rows_here, columns).astype(jnp.bfloat16)
        if level_bit == 0:
            back = from_partner(jnp.concatenate([key_back, value_back], 1), "seq", level_bit)
            back_keys = back[:, :columns]
            back_values = back[:, columns:]
        else:
            back_values = from_partner(value_back, "seq", level_bit)
            back_keys = from_partner(key_back, "seq", level_bit)
        key_sum = key_sum + split(back_keys).astype(jnp.float32)
        value_sum = value_sum + split(back_values).astype(jnp.float32)
    global_product = jnp.einsum(
        "thd,ghd->htg", dout_heads, split(global_values), preferred_element_type=jnp.float32
    )
    global_slope = (global_prob * (global_product - delta[:, :, None])).astype(jnp.bfloat16)
    query_sum = query_sum + jnp.einsum(
        "htg,ghd->thd", global_slope, split(global_keys), preferred_element_type=jnp.float32
    )
    key_part = jnp.einsum(
        "htg,thd->ghd", global_slope, query_heads, preferred_element_type=jnp.float32
    )
    value_part = jnp.einsum(
        "htg,thd->ghd", global_prob_b, dout_heads, preferred_element_type=jnp.float32
    )
    owned = jnp.concatenate(
        [key_part.reshape(global_count, columns), value_part.reshape(global_count, columns)], 1
    )
    for bit in owner_bits:
        half = owned.shape[0] // 2
        owned = owned[:half] + from_partner(owned[half:], "seq", bit)
    owned = jnp.concatenate([temper * owned[:, :columns], owned[:, columns:]], 1)
    placement = (jnp.arange(rows_here, dtype=jnp.int32)[:, None] == global_offsets[None, :]).astype(
        jnp.float32
    )
    spread_rows = jnp.dot(
        placement, owned, precision=lax.Precision.HIGHEST, preferred_element_type=jnp.float32
    )
    key_grad = (key_sum.reshape(rows_here, columns) + spread_rows[:, :columns]).astype(jnp.bfloat16)
    value_grad = (value_sum.reshape(rows_here, columns) + spread_rows[:, columns:]).astype(
        jnp.bfloat16
    )
    query_grad = (temper * query_sum).reshape(rows_here, columns).astype(jnp.bfloat16)
    return (attended, query_grad, key_grad, value_grad)


def solution(mesh):
    in_specs = (
        P(("dp", "seq"), None),
        P(("dp", "seq"), None),
        P(("dp", "seq"), None),
        P(("dp", "seq"), None),
        P(("dp", "seq")),
        P(("dp", "seq")),
    )
    out_specs = (
        P(("dp", "seq"), None),
        P(("dp", "seq"), None),
        P(("dp", "seq"), None),
        P(("dp", "seq"), None),
    )
    return jax.shard_map(body, mesh=mesh, in_specs=in_specs, out_specs=out_specs, check_vma=False)
```

```python
import jax
import jax.numpy as jnp
from jax import lax
from jax.sharding import PartitionSpec as P

HEADS = 16
LEVELS = 2


def from_partner(array, axis, stride):
    return lax.ppermute(array, axis, [(i, i ^ 1 << stride) for i in range(lax.axis_size(axis))])


def body(queries, keys, values, cotangent, documents, global_offsets):
    rows_here, columns = queries.shape
    head_size = columns // HEADS
    temper = head_size ** (-0.5)
    shards = lax.axis_size("seq")
    log_shards = shards.bit_length() - 1
    level_bits = [step * (log_shards - 2) // (LEVELS - 1) for step in range(LEVELS)]

    def split(array):
        return array.reshape(array.shape[0], HEADS, head_size)

    per_block = global_offsets.shape[0]
    picked = jnp.stack(
        [
            jnp.concatenate(
                [lax.dynamic_slice_in_dim(array, global_offsets[j], 1) for j in range(per_block)], 0
            )
            for array in (keys, values)
        ],
        0,
    )
    gather_bits = list(range(log_shards))[::-1]
    z_steps = min(3, log_shards)
    doc_columns = 128
    packed = jnp.concatenate(
        [keys, values, jnp.broadcast_to(documents.astype(keys.dtype)[:, None], (rows_here, doc_columns))],
        1,
    )
    gathered = picked
    arrived = {}
    for step, bit in enumerate(gather_bits):
        gathered = jnp.stack([gathered, from_partner(gathered, "seq", bit)], 0)
        if step == z_steps - 1:
            gathered, held = lax.optimization_barrier((gathered, packed))
            for level_bit in level_bits:
                arrived[level_bit] = from_partner(held, "seq", level_bit)
    owner_bits = gather_bits[::-1]
    global_count = shards * per_block
    gathered = gathered.reshape((shards,) + picked.shape)
    global_keys = gathered[:, 0].reshape(global_count, columns)
    global_values = gathered[:, 1].reshape(global_count, columns)
    slot = jnp.arange(shards, dtype=jnp.int32)
    distance = jnp.zeros_like(slot)
    for position, bit in enumerate(owner_bits):
        distance = distance | (((slot >> (log_shards - 1 - position)) & 1) << bit)
    distance = jnp.repeat(distance, per_block)
    nearby = distance == 0
    for level_bit in level_bits:
        nearby = nearby | (distance == 1 << level_bit)
    query_heads = split(queries)
    dout_heads = split(cotangent)
    key_list = [keys]
    value_list = [values]
    mask_list = [documents[:, None] == documents[None, :]]
    for level_bit in level_bits:
        came = arrived[level_bit]
        partner_keys = came[:, :columns]
        partner_values = came[:, columns : 2 * columns]
        partner_docs = came[:, 2 * columns].astype(documents.dtype)
        key_list.append(partner_keys)
        value_list.append(partner_values)
        mask_list.append(documents[:, None] == partner_docs[None, :])
    block_keys = jnp.concatenate(key_list, 0)
    block_values = jnp.concatenate(value_list, 0)
    block_mask = jnp.concatenate(mask_list, 1)
    raws = [
        jnp.einsum("thd,uhd->htu", query_heads, split(group), preferred_element_type=jnp.float32)
        for group in key_list
    ]
    products = [
        jnp.einsum("thd,uhd->htu", dout_heads, split(group), preferred_element_type=jnp.float32)
        for group in value_list
    ]
    early = [0] + [level + 1 for level, level_bit in enumerate(level_bits) if level_bit == 0]
    held = lax.optimization_barrier(([raws[i] for i in early], [products[i] for i in early]))
    for position, i in enumerate(early):
        raws[i] = held[0][position]
        products[i] = held[1][position]
    raw = jnp.concatenate(raws, 2) * temper
    block_scores = jnp.where(block_mask[None], raw, -jnp.inf)
    global_raw = (
        jnp.einsum(
            "thd,ghd->htg", query_heads, split(global_keys), preferred_element_type=jnp.float32
        )
        * temper
    )
    global_scores = jnp.where(jnp.logical_not(nearby)[None, None, :], global_raw, -jnp.inf)
    highest = jnp.maximum(jnp.max(global_scores, axis=-1), jnp.max(block_scores, axis=-1))
    block_exp = jnp.exp(block_scores - highest[..., None])
    global_exp = jnp.exp(global_scores - highest[..., None])
    totals = jnp.sum(global_exp, axis=-1) + jnp.sum(block_exp, axis=-1)
    probs = block_exp / totals[..., None]
    global_prob = global_exp / totals[..., None]
    probs_b = probs.astype(jnp.bfloat16)
    global_prob_b = global_prob.astype(jnp.bfloat16)
    summed = jnp.einsum(
        "htg,ghd->thd", global_prob_b, split(global_values), preferred_element_type=jnp.float32
    )
    summed = summed + jnp.einsum(
        "htu,uhd->thd", probs_b, split(block_values), preferred_element_type=jnp.float32
    )
    attended = summed.astype(jnp.bfloat16).reshape(rows_here, columns)
    delta = jnp.sum(dout_heads.astype(jnp.float32) * split(attended).astype(jnp.float32), axis=-1).T
    product = jnp.concatenate(products, 2)
    slope = (probs * (product - delta[:, :, None])).astype(jnp.bfloat16)
    query_term = jnp.einsum(
        "htu,uhd->thd", slope, split(block_keys), preferred_element_type=jnp.float32
    )
    key_term = temper * jnp.einsum(
        "htu,thd->uhd", slope, query_heads, preferred_element_type=jnp.float32
    )
    value_term = jnp.einsum("htu,thd->uhd", probs_b, dout_heads, preferred_element_type=jnp.float32)
    query_sum = query_term
    key_sum = key_term[:rows_here]
    value_sum = value_term[:rows_here]
    for level, level_bit in enumerate(level_bits):
        lower = (level + 1) * rows_here
        upper = (level + 2) * rows_here
        key_back = key_term[lower:upper].reshape(rows_here, columns).astype(jnp.bfloat16)
        value_back = value_term[lower:upper].reshape(rows_here, columns).astype(jnp.bfloat16)
        if level_bit == 0:
            back = from_partner(jnp.concatenate([key_back, value_back], 1), "seq", level_bit)
            back_keys = back[:, :columns]
            back_values = back[:, columns:]
        else:
            back_values = from_partner(value_back, "seq", level_bit)
            back_keys = from_partner(key_back, "seq", level_bit)
        key_sum = key_sum + split(back_keys).astype(jnp.float32)
        value_sum = value_sum + split(back_values).astype(jnp.float32)
    global_product = jnp.einsum(
        "thd,ghd->htg", dout_heads, split(global_values), preferred_element_type=jnp.float32
    )
    global_slope = (global_prob * (global_product - delta[:, :, None])).astype(jnp.bfloat16)
    query_sum = query_sum + jnp.einsum(
        "htg,ghd->thd", global_slope, split(global_keys), preferred_element_type=jnp.float32
    )
    key_part = jnp.einsum(
        "htg,thd->ghd", global_slope, query_heads, preferred_element_type=jnp.float32
    )
    value_part = jnp.einsum(
        "htg,thd->ghd", global_prob_b, dout_heads, preferred_element_type=jnp.float32
    )
    owned = jnp.concatenate(
        [key_part.reshape(global_count, columns), value_part.reshape(global_count, columns)], 1
    )
    for bit in owner_bits:
        half = owned.shape[0] // 2
        owned = owned[:half] + from_partner(owned[half:], "seq", bit)
    owned = jnp.concatenate([temper * owned[:, :columns], owned[:, columns:]], 1)
    positions = jnp.arange(rows_here, dtype=jnp.int32)[:, None]
    spread_rows = jnp.zeros((rows_here, 2 * columns), jnp.float32)
    for j in range(per_block):
        spread_rows = spread_rows + jnp.where(
            positions == global_offsets[j], owned[j][None, :], 0.0
        )
    key_grad = (key_sum.reshape(rows_here, columns) + spread_rows[:, :columns]).astype(jnp.bfloat16)
    value_grad = (value_sum.reshape(rows_here, columns) + spread_rows[:, columns:]).astype(
        jnp.bfloat16
    )
    query_grad = (temper * query_sum).reshape(rows_here, columns).astype(jnp.bfloat16)
    return (attended, query_grad, key_grad, value_grad)


def solution(mesh):
    in_specs = (
        P(("dp", "seq"), None),
        P(("dp", "seq"), None),
        P(("dp", "seq"), None),
        P(("dp", "seq"), None),
        P(("dp", "seq")),
        P(("dp", "seq")),
    )
    out_specs = (
        P(("dp", "seq"), None),
        P(("dp", "seq"), None),
        P(("dp", "seq"), None),
        P(("dp", "seq"), None),
    )
    return jax.shard_map(body, mesh=mesh, in_specs=in_specs, out_specs=out_specs, check_vma=False)
```

```python
import jax
import jax.numpy as jnp
from jax import lax
from jax.sharding import PartitionSpec as P

HEADS = 16
LEVELS = 2


def from_partner(array, axis, stride):
    return lax.ppermute(array, axis, [(i, i ^ 1 << stride) for i in range(lax.axis_size(axis))])


def body(queries, keys, values, cotangent, documents, global_offsets):
    rows_here, columns = queries.shape
    head_size = columns // HEADS
    temper = head_size ** (-0.5)
    shards = lax.axis_size("seq")
    log_shards = shards.bit_length() - 1
    level_bits = [step * (log_shards - 2) // (LEVELS - 1) for step in range(LEVELS)]

    def split(array):
        return array.reshape(array.shape[0], HEADS, head_size)

    per_block = global_offsets.shape[0]
    chooser = (
        global_offsets[:, None] == jnp.arange(rows_here, dtype=global_offsets.dtype)[None, :]
    ).astype(keys.dtype)
    picked = jnp.stack(
        [
            jnp.dot(chooser, array, preferred_element_type=jnp.float32).astype(array.dtype)
            for array in (keys, values)
        ],
        0,
    )
    gather_bits = list(range(log_shards))[::-1]
    z_steps = min(3, log_shards)
    doc_columns = 128
    packed = jnp.concatenate(
        [keys, values, jnp.broadcast_to(documents.astype(keys.dtype)[:, None], (rows_here, doc_columns))],
        1,
    )
    gathered = picked
    arrived = {}
    for step, bit in enumerate(gather_bits):
        gathered = jnp.stack([gathered, from_partner(gathered, "seq", bit)], 0)
        if step == z_steps - 1:
            gathered, held = lax.optimization_barrier((gathered, packed))
            for level_bit in level_bits:
                arrived[level_bit] = from_partner(held, "seq", level_bit)
    owner_bits = gather_bits[::-1]
    global_count = shards * per_block
    gathered = gathered.reshape((shards,) + picked.shape)
    global_keys = gathered[:, 0].reshape(global_count, columns)
    global_values = gathered[:, 1].reshape(global_count, columns)
    slot = jnp.arange(shards, dtype=jnp.int32)
    distance = jnp.zeros_like(slot)
    for position, bit in enumerate(owner_bits):
        distance = distance | (((slot >> (log_shards - 1 - position)) & 1) << bit)
    distance = jnp.repeat(distance, per_block)
    nearby = distance == 0
    for level_bit in level_bits:
        nearby = nearby | (distance == 1 << level_bit)
    query_heads = split(queries)
    dout_heads = split(cotangent)
    key_list = [keys]
    value_list = [values]
    mask_list = [documents[:, None] == documents[None, :]]
    for level_bit in level_bits:
        came = arrived[level_bit]
        partner_keys = came[:, :columns]
        partner_values = came[:, columns : 2 * columns]
        partner_docs = came[:, 2 * columns].astype(documents.dtype)
        key_list.append(partner_keys)
        value_list.append(partner_values)
        mask_list.append(documents[:, None] == partner_docs[None, :])
    block_keys = jnp.concatenate(key_list, 0)
    block_values = jnp.concatenate(value_list, 0)
    block_mask = jnp.concatenate(mask_list, 1)
    raws = [
        jnp.einsum("thd,uhd->htu", query_heads, split(group), preferred_element_type=jnp.float32)
        for group in key_list
    ]
    products = [
        jnp.einsum("thd,uhd->htu", dout_heads, split(group), preferred_element_type=jnp.float32)
        for group in value_list
    ]
    early = [0] + [level + 1 for level, level_bit in enumerate(level_bits) if level_bit == 0]
    held = lax.optimization_barrier(([raws[i] for i in early], [products[i] for i in early]))
    for position, i in enumerate(early):
        raws[i] = held[0][position]
        products[i] = held[1][position]
    raw = jnp.concatenate(raws, 2) * temper
    block_scores = jnp.where(block_mask[None], raw, -jnp.inf)
    global_raw = (
        jnp.einsum(
            "thd,ghd->htg", query_heads, split(global_keys), preferred_element_type=jnp.float32
        )
        * temper
    )
    global_scores = jnp.where(jnp.logical_not(nearby)[None, None, :], global_raw, -jnp.inf)
    highest = jnp.maximum(jnp.max(global_scores, axis=-1), jnp.max(block_scores, axis=-1))
    block_exp = jnp.exp(block_scores - highest[..., None])
    global_exp = jnp.exp(global_scores - highest[..., None])
    totals = jnp.sum(global_exp, axis=-1) + jnp.sum(block_exp, axis=-1)
    probs = block_exp / totals[..., None]
    global_prob = global_exp / totals[..., None]
    probs_b = probs.astype(jnp.bfloat16)
    global_prob_b = global_prob.astype(jnp.bfloat16)
    summed = jnp.einsum(
        "htg,ghd->thd", global_prob_b, split(global_values), preferred_element_type=jnp.float32
    )
    summed = summed + jnp.einsum(
        "htu,uhd->thd", probs_b, split(block_values), preferred_element_type=jnp.float32
    )
    attended = summed.astype(jnp.bfloat16).reshape(rows_here, columns)
    delta = jnp.sum(dout_heads.astype(jnp.float32) * split(attended).astype(jnp.float32), axis=-1).T
    product = jnp.concatenate(products, 2)
    slope = (probs * (product - delta[:, :, None])).astype(jnp.bfloat16)
    query_term = jnp.einsum(
        "htu,uhd->thd", slope, split(block_keys), preferred_element_type=jnp.float32
    )
    key_term = temper * jnp.einsum(
        "htu,thd->uhd", slope, query_heads, preferred_element_type=jnp.float32
    )
    value_term = jnp.einsum("htu,thd->uhd", probs_b, dout_heads, preferred_element_type=jnp.float32)
    query_sum = query_term
    key_sum = key_term[:rows_here]
    value_sum = value_term[:rows_here]
    for level, level_bit in enumerate(level_bits):
        lower = (level + 1) * rows_here
        upper = (level + 2) * rows_here
        key_back = key_term[lower:upper].reshape(rows_here, columns).astype(jnp.bfloat16)
        value_back = value_term[lower:upper].reshape(rows_here, columns).astype(jnp.bfloat16)
        if level_bit == 0:
            back = from_partner(jnp.concatenate([key_back, value_back], 1), "seq", level_bit)
            back_keys = back[:, :columns]
            back_values = back[:, columns:]
        else:
            back_values = from_partner(value_back, "seq", level_bit)
            back_keys = from_partner(key_back, "seq", level_bit)
        key_sum = key_sum + split(back_keys).astype(jnp.float32)
        value_sum = value_sum + split(back_values).astype(jnp.float32)
    global_product = jnp.einsum(
        "thd,ghd->htg", dout_heads, split(global_values), preferred_element_type=jnp.float32
    )
    global_slope = (global_prob * (global_product - delta[:, :, None])).astype(jnp.bfloat16)
    query_sum = query_sum + jnp.einsum(
        "htg,ghd->thd", global_slope, split(global_keys), preferred_element_type=jnp.float32
    )
    key_part = jnp.einsum(
        "htg,thd->ghd", global_slope, query_heads, preferred_element_type=jnp.float32
    )
    value_part = jnp.einsum(
        "htg,thd->ghd", global_prob_b, dout_heads, preferred_element_type=jnp.float32
    )
    owned = jnp.concatenate(
        [key_part.reshape(global_count, columns), value_part.reshape(global_count, columns)], 1
    )
    for bit in owner_bits:
        half = owned.shape[0] // 2
        sent = owned[half:]
        sent = sent.astype(jnp.bfloat16)
        owned = owned[:half] + from_partner(sent, "seq", bit).astype(jnp.float32)
    owned = jnp.concatenate([temper * owned[:, :columns], owned[:, columns:]], 1)
    placement = (jnp.arange(rows_here, dtype=jnp.int32)[:, None] == global_offsets[None, :]).astype(
        jnp.float32
    )
    spread_rows = jnp.dot(
        placement, owned, precision=lax.Precision.HIGHEST, preferred_element_type=jnp.float32
    )
    key_grad = (key_sum.reshape(rows_here, columns) + spread_rows[:, :columns]).astype(jnp.bfloat16)
    value_grad = (value_sum.reshape(rows_here, columns) + spread_rows[:, columns:]).astype(
        jnp.bfloat16
    )
    query_grad = (temper * query_sum).reshape(rows_here, columns).astype(jnp.bfloat16)
    return (attended, query_grad, key_grad, value_grad)


def solution(mesh):
    in_specs = (
        P(("dp", "seq"), None),
        P(("dp", "seq"), None),
        P(("dp", "seq"), None),
        P(("dp", "seq"), None),
        P(("dp", "seq")),
        P(("dp", "seq")),
    )
    out_specs = (
        P(("dp", "seq"), None),
        P(("dp", "seq"), None),
        P(("dp", "seq"), None),
        P(("dp", "seq"), None),
    )
    return jax.shard_map(body, mesh=mesh, in_specs=in_specs, out_specs=out_specs, check_vma=False)
```
